128 devices in a mesh: loop: 8 (over x_hi, z), long: 16 (over y, x_lo, core).
Axes of the slice: x: 4 (x_hi: 2, x_lo: 2; x = x_hi * 2 + x_lo), y: 4, z: 4, core: 2. Of those that a mesh axis runs over, the one named last changes fastest.
Arguments:
- amplitudes: bfloat16 [19200, 8192], P('long', 'loop'), may hold values from -6 to 6
- integrals: bfloat16 [19200, 6400], P('long', 'loop'), may hold values from -0.046875 to 0.046875
- owner: int32 [128], replicated, may hold values from 0 to 15, as said below
Outputs:
- residual: float32 [6400, 8192], P('long', 'loop')
The draws below stay inside these ranges and needn't reach their ends.
Inputs may be any that keep to these rules, and one draw needn't show every extreme that they name: Each slab of 16 consecutive tiles names every owner exactly once.
All inputs are finite; a program needn't handle non-finite values.
Results may differ from the reference program's by a relative error of at most 0.0003.
Values may be sent and summed in bfloat16 or wider, within the bound.
No kernel may reach another device: no remote copies, remote signals or barrier semaphores. Data moves between devices by JAX's collectives and lax.ppermute only.
A program may use at most 192 MiB of HBM per device.

```python
import jax
import jax.numpy as jnp
from jax import lax

TB = 50
TPS = 1
K = 19200
TILES_SLAB = 16
NTILE = 128
AB = 6400
P_SIZE = 8192


def draw_owner(key, part):
    repeated = jnp.arange(TILES_SLAB, dtype=jnp.int32) // TPS
    slab_keys = jax.random.split(key, NTILE // TILES_SLAB)

    def shuffle(slab_key):
        return jax.random.permutation(slab_key, repeated)
    return jax.vmap(shuffle)(slab_keys).reshape(-1).astype(jnp.int32)


def levels(stream_key, shape, cuts, least, top_value):
    gain = 1.0
    for dim, shards_of in cuts:
        draws = jax.random.uniform(jax.random.fold_in(jax.random.fold_in(stream_key, 6), dim), (shards_of,), jnp.float32, least / len(cuts), top_value / len(cuts))
        gain = gain * jnp.repeat(jnp.exp(draws), shape[dim] // shards_of).reshape((-1,) + (1,) * (len(shape) - 1 - dim))
    return gain


def noise(stream_key, extent, spread, bound, cuts=(), kind=jnp.bfloat16):
    result = jax.random.normal(stream_key, extent, jnp.float32) * spread
    if len(cuts) > 0:
        result = levels(stream_key, extent, cuts, -0.22, 0.18) * result
    return jnp.clip(result, min=-bound, max=bound).astype(kind)


def setup_inputs(seed: int = 0) -> dict:
    keys = jax.random.split(jax.random.key(seed), 4)
    amplitudes = noise(keys[0], (K, P_SIZE), 1.0, 6.0, ((0, 16), (1, 8)))
    integrals = noise(keys[1], (K, AB), K ** -0.5, 0.046875, ((0, 16), (1, 8)))
    owner = draw_owner(jax.random.fold_in(keys[3], 71), 0)
    return {"amplitudes": amplitudes, "integrals": integrals, "owner": owner}


def reference(amplitudes, integrals, owner):
    tile_count = owner.shape[0]
    ladder = lax.dot_general(integrals, amplitudes, (((0,), (0,)), ((), ())), preferred_element_type=jnp.float32)
    slot_order = jnp.argsort(owner * tile_count + jnp.arange(tile_count, dtype=jnp.int32))
    tile_view = ladder.reshape(tile_count, TB, ladder.shape[1])
    return jnp.take(tile_view, slot_order, axis=0).reshape(tile_count * TB, ladder.shape[1])
```

```python
import jax
import jax.numpy as jnp
from jax import lax
from jax.sharding import Mesh
from jax.sharding import PartitionSpec as P

TB = 50
LOOP_AXES = ("xh", "z")
LONG_AXES = ("y", "xl", "c")


def local(amplitudes, integrals, owner):
    nxh = lax.axis_size("xh")
    nz = lax.axis_size("z")
    nc = lax.axis_size("c")
    kc = integrals.shape[0]
    tiles_slab = integrals.shape[1] // TB
    slab = lax.axis_index("xh") * nz + lax.axis_index("z")

    slab_owner = lax.dynamic_slice(owner, (slab * tiles_slab,), (tiles_slab,))
    position = jnp.argsort(slab_owner)
    tiles = integrals.reshape(kc, tiles_slab, TB)
    by_owner = jnp.take(tiles, position, axis=1)
    by_owner = by_owner.reshape(kc, tiles_slab // nc, nc, TB)
    by_owner = jnp.moveaxis(by_owner, 2, 0)

    mine = lax.all_to_all(by_owner, "c", 0, 0, tiled=True)
    mine = mine.reshape(nc * kc, tiles_slab // nc, TB)
    gathered = lax.all_gather(mine, "z", axis=0, tiled=False)

    amp = lax.all_gather(amplitudes, "xh", axis=1, tiled=True)
    amp = lax.all_gather(amp, "c", axis=0, tiled=True)

    partial = jnp.einsum(
        "zqkr,qn->kzrn", gathered, amp, preferred_element_type=jnp.float32
    )
    partial = partial.reshape(-1, partial.shape[-1])
    summed = lax.psum_scatter(partial, ("y", "xl"), scatter_dimension=0, tiled=True)
    summed = summed.reshape(nz, TB, nxh, amplitudes.shape[1])
    out = lax.all_to_all(summed, "xh", 2, 0, tiled=True)
    return out.reshape(nxh * nz * TB, amplitudes.shape[1])


def solution(mesh):
    n_loop, n_long = mesh.devices.shape
    fine = Mesh(
        mesh.devices.reshape(2, n_loop // 2, n_long // 4, 2, 2), LOOP_AXES + LONG_AXES
    )
    placed = P(LONG_AXES, LOOP_AXES)
    return jax.shard_map(
        local,
        mesh=fine,
        in_specs=(placed, placed, P()),
        out_specs=placed,
        check_vma=False,
    )
```

```python
import jax
import jax.numpy as jnp
from jax import lax
from jax.sharding import Mesh
from jax.sharding import PartitionSpec as P

TB = 50
LOOP_AXES = ("xh", "z")
LONG_AXES = ("y", "xl", "c")
SWAP = [(0, 1), (1, 0)]


def local(amplitudes, integrals, owner):
    nz = lax.axis_size("z")
    kc = integrals.shape[0]
    width = amplitudes.shape[1]
    tiles_slab = integrals.shape[1] // TB
    xh = lax.axis_index("xh")
    core = lax.axis_index("c")
    slab = xh * nz + lax.axis_index("z")

    slab_owner = lax.dynamic_slice(owner, (slab * tiles_slab,), (tiles_slab,))
    position = jnp.argsort(slab_owner).reshape(tiles_slab // 2, 2)
    tiles = integrals.reshape(kc, tiles_slab, TB)
    mine = jnp.take(tiles, position[:, core], axis=1)
    theirs = jnp.take(tiles, position[:, 1 - core], axis=1)
    from_sibling = lax.ppermute(theirs, "c", SWAP)
    own_owners = jnp.concatenate([mine, from_sibling], axis=0)
    gathered = lax.all_gather(own_owners, "z", axis=0, tiled=False)
    lhs = jnp.transpose(gathered, (1, 2, 0, 3)).reshape(2 * kc, -1)

    amp = jnp.concatenate([amplitudes, lax.ppermute(amplitudes, "xh", SWAP)], axis=1)
    amp = jnp.concatenate([amp, lax.ppermute(amp, "c", SWAP)], axis=0)

    partial = lax.dot_general(
        lhs, amp, (((0,), (0,)), ((), ())), preferred_element_type=jnp.float32
    )
    summed = lax.psum_scatter(partial, ("y", "xl"), scatter_dimension=0, tiled=True)
    keep = summed[:, :width]
    recv = lax.ppermute(summed[:, width:], "xh", SWAP)
    return jnp.where(
        xh == 0,
        jnp.concatenate([keep, recv], axis=0),
        jnp.concatenate([recv, keep], axis=0),
    )


def solution(mesh):
    n_loop, n_long = mesh.devices.shape
    fine = Mesh(
        mesh.devices.reshape(2, n_loop // 2, n_long // 4, 2, 2), LOOP_AXES + LONG_AXES
    )
    placed = P(LONG_AXES, LOOP_AXES)
    return jax.shard_map(
        local,
        mesh=fine,
        in_specs=(placed, placed, P()),
        out_specs=placed,
        check_vma=False,
    )
```

```python
import jax
import jax.numpy as jnp
from jax import lax
from jax.sharding import Mesh
from jax.sharding import PartitionSpec as P

TB = 50
LOOP_AXES = ("xh", "z")
LONG_AXES = ("y", "xl", "c")
SWAP = [(0, 1), (1, 0)]


def local(amplitudes, integrals, owner):
    nz = lax.axis_size("z")
    kc = integrals.shape[0]
    width = amplitudes.shape[1]
    tiles_slab = integrals.shape[1] // TB
    xh = lax.axis_index("xh")
    core = lax.axis_index("c")
    slab = xh * nz + lax.axis_index("z")

    slab_owner = lax.dynamic_slice(owner, (slab * tiles_slab,), (tiles_slab,))
    position = jnp.argsort(slab_owner).reshape(tiles_slab // 2, 2)
    tiles = integrals.T.reshape(tiles_slab, TB, kc)
    mine = jnp.take(tiles, position[:, core], axis=0)
    theirs = jnp.take(tiles, position[:, 1 - core], axis=0)
    from_sibling = lax.ppermute(theirs, "c", SWAP)
    own_owners = jnp.stack([mine, from_sibling], axis=2)
    gathered = lax.all_gather(own_owners, "z", axis=1, tiled=True)

    amp = jnp.concatenate([amplitudes, lax.ppermute(amplitudes, "xh", SWAP)], axis=1)
    amp = jnp.stack([amp, lax.ppermute(amp, "c", SWAP)], axis=0)

    partial = lax.dot_general(
        gathered, amp, (((2, 3), (0, 1)), ((), ())), preferred_element_type=jnp.float32
    )
    partial = partial.reshape(-1, partial.shape[-1])
    summed = lax.psum_scatter(partial, ("y", "xl"), scatter_dimension=0, tiled=True)
    keep = summed[:, :width]
    recv = lax.ppermute(summed[:, width:], "xh", SWAP)
    return jnp.where(
        xh == 0,
        jnp.concatenate([keep, recv], axis=0),
        jnp.concatenate([recv, keep], axis=0),
    )


def solution(mesh):
    n_loop, n_long = mesh.devices.shape
    fine = Mesh(
        mesh.devices.reshape(2, n_loop // 2, n_long // 4, 2, 2), LOOP_AXES + LONG_AXES
    )
    placed = P(LONG_AXES, LOOP_AXES)
    return jax.shard_map(
        local,
        mesh=fine,
        in_specs=(placed, placed, P()),
        out_specs=placed,
        check_vma=False,
    )
```

```python
import jax
import jax.numpy as jnp
from jax import lax
from jax.sharding import Mesh
from jax.sharding import PartitionSpec as P

TB = 50
LOOP_AXES = ("xh", "z")
LONG_AXES = ("y", "xl", "c")
SWAP = [(0, 1), (1, 0)]


def ring_pick(parts, index):
    return lax.dynamic_index_in_dim(parts, index % parts.shape[0], 0, keepdims=False)


def reduce_scatter_y_then_xl(partial):
    ny = lax.axis_size("y")
    nxl = lax.axis_size("xl")
    yi = lax.axis_index("y")
    xi = lax.axis_index("xl")
    rows = partial.shape[0] // (ny * nxl)
    half = rows // 2
    parts = partial.reshape(ny, nxl, rows, partial.shape[1])
    ahead, back = parts[:, :, :half], parts[:, :, half:]
    to_next = [(i, (i + 1) % ny) for i in range(ny)]
    to_prev = [(i, (i - 1) % ny) for i in range(ny)]
    acc_ahead = ring_pick(ahead, yi + ny - 1)
    acc_back = ring_pick(back, yi + 1)
    for step in range(ny - 1):
        got_ahead = lax.ppermute(acc_ahead, "y", to_next)
        got_back = lax.ppermute(acc_back, "y", to_prev)
        acc_ahead = got_ahead + ring_pick(ahead, yi + 2 * ny - 2 - step)
        acc_back = got_back + ring_pick(back, yi + 2 + step)
    done = jnp.concatenate([acc_ahead, acc_back], axis=1)
    mine = lax.dynamic_index_in_dim(done, xi, 0, keepdims=False)
    other = lax.dynamic_index_in_dim(done, 1 - xi, 0, keepdims=False)
    return mine + lax.ppermute(other, "xl", SWAP)


def local(amplitudes, integrals, owner):
    nz = lax.axis_size("z")
    kc = integrals.shape[0]
    width = amplitudes.shape[1]
    tiles_slab = integrals.shape[1] // TB
    xh = lax.axis_index("xh")
    core = lax.axis_index("c")
    slab = xh * nz + lax.axis_index("z")

    slab_owner = lax.dynamic_slice(owner, (slab * tiles_slab,), (tiles_slab,))
    position = jnp.argsort(slab_owner).reshape(tiles_slab // 2, 2)
    tiles = integrals.T.reshape(tiles_slab, TB, kc)
    mine = jnp.take(tiles, position[:, core], axis=0)
    theirs = jnp.take(tiles, position[:, 1 - core], axis=0)
    from_sibling = lax.ppermute(theirs, "c", SWAP)
    own_owners = jnp.stack([mine, from_sibling], axis=2)
    gathered = lax.all_gather(own_owners, "z", axis=1, tiled=True)

    amp = jnp.concatenate([amplitudes, lax.ppermute(amplitudes, "xh", SWAP)], axis=1)
    amp = jnp.stack([amp, lax.ppermute(amp, "c", SWAP)], axis=0)

    partial = lax.dot_general(
        gathered, amp, (((2, 3), (0, 1)), ((), ())), preferred_element_type=jnp.float32
    )
    partial = partial.reshape(-1, partial.shape[-1])
    summed = reduce_scatter_y_then_xl(partial)
    keep = summed[:, :width]
    recv = lax.ppermute(summed[:, width:], "xh", SWAP)
    return jnp.where(
        xh == 0,
        jnp.concatenate([keep, recv], axis=0),
        jnp.concatenate([recv, keep], axis=0),
    )


def solution(mesh):
    n_loop, n_long = mesh.devices.shape
    fine = Mesh(
        mesh.devices.reshape(2, n_loop // 2, n_long // 4, 2, 2), LOOP_AXES + LONG_AXES
    )
    placed = P(LONG_AXES, LOOP_AXES)
    return jax.shard_map(
        local,
        mesh=fine,
        in_specs=(placed, placed, P()),
        out_specs=placed,
        check_vma=False,
    )
```

```python
import jax
import jax.numpy as jnp
from jax import lax
from jax.sharding import Mesh
from jax.sharding import PartitionSpec as P

TB = 50
LOOP_AXES = ("xh", "z")
LONG_AXES = ("y", "xl", "c")
SWAP = [(0, 1), (1, 0)]


def local(amplitudes, integrals, owner):
    nz = lax.axis_size("z")
    ny = lax.axis_size("y")
    nxl = lax.axis_size("xl")
    kc = integrals.shape[0]
    width = amplitudes.shape[1]
    tiles_slab = integrals.shape[1] // TB
    xh = lax.axis_index("xh")
    yi = lax.axis_index("y")
    xi = lax.axis_index("xl")
    core = lax.axis_index("c")
    slab = xh * nz + lax.axis_index("z")

    slab_owner = lax.dynamic_slice(owner, (slab * tiles_slab,), (tiles_slab,))
    position = jnp.argsort(slab_owner).reshape(tiles_slab // 2, 2)
    tiles = integrals.T.reshape(tiles_slab, TB, kc)
    mine = jnp.take(tiles, position[:, core], axis=0)
    theirs = jnp.take(tiles, position[:, 1 - core], axis=0)
    from_sibling = lax.ppermute(theirs, "c", SWAP)
    own_owners = jnp.stack([mine, from_sibling], axis=2)
    gathered = lax.all_gather(own_owners, "z", axis=1, tiled=True)
    rows = gathered.shape[1]
    half = rows // 2
    by_y = gathered.reshape(ny, nxl, rows, 2, kc)

    amp = jnp.concatenate([amplitudes, lax.ppermute(amplitudes, "xh", SWAP)], axis=1)
    amp = jnp.stack([amp, lax.ppermute(amp, "c", SWAP)], axis=0)

    def block(y_owner, part):
        lhs = lax.dynamic_index_in_dim(by_y, y_owner % ny, 0, keepdims=False)
        lhs = lhs[:, part * half : (part + 1) * half]
        return lax.dot_general(
            lhs, amp, (((2, 3), (0, 1)), ((), ())), preferred_element_type=jnp.float32
        )

    to_next = [(i, (i + 1) % ny) for i in range(ny)]
    to_prev = [(i, (i - 1) % ny) for i in range(ny)]
    acc_ahead = block(yi + ny - 1, 0)
    acc_back = block(yi + 1, 1)
    for step in range(ny - 1):
        got_ahead = lax.ppermute(acc_ahead, "y", to_next)
        got_back = lax.ppermute(acc_back, "y", to_prev)
        acc_ahead = got_ahead + block(yi + 2 * ny - 2 - step, 0)
        acc_back = got_back + block(yi + 2 + step, 1)

    kept, came = [], []
    for acc in (acc_ahead, acc_back):
        here = lax.dynamic_index_in_dim(acc, xi, 0, keepdims=False)
        there = lax.dynamic_index_in_dim(acc, 1 - xi, 0, keepdims=False)
        summed = here + lax.ppermute(there, "xl", SWAP)
        kept.append(summed[:, :width])
        came.append(lax.ppermute(summed[:, width:], "xh", SWAP))
    first = jnp.concatenate(kept + came, axis=0)
    second = jnp.concatenate(came + kept, axis=0)
    return jnp.where(xh == 0, first, second)


def solution(mesh):
    n_loop, n_long = mesh.devices.shape
    fine = Mesh(
        mesh.devices.reshape(2, n_loop // 2, n_long // 4, 2, 2), LOOP_AXES + LONG_AXES
    )
    placed = P(LONG_AXES, LOOP_AXES)
    return jax.shard_map(
        local,
        mesh=fine,
        in_specs=(placed, placed, P()),
        out_specs=placed,
        check_vma=False,
    )
```

```python
import jax
import jax.numpy as jnp
from jax import lax
from jax.sharding import Mesh
from jax.sharding import PartitionSpec as P

TB = 50
LOOP_AXES = ("xh", "z")
LONG_AXES = ("y", "xl", "c")
SWAP = [(0, 1), (1, 0)]


def local(amplitudes, integrals, owner):
    nz = lax.axis_size("z")
    ny = lax.axis_size("y")
    nxl = lax.axis_size("xl")
    kc = integrals.shape[0]
    width = amplitudes.shape[1]
    tiles_slab = integrals.shape[1] // TB
    xh = lax.axis_index("xh")
    yi = lax.axis_index("y")
    xi = lax.axis_index("xl")
    core = lax.axis_index("c")
    slab = xh * nz + lax.axis_index("z")

    slab_owner = lax.dynamic_slice(owner, (slab * tiles_slab,), (tiles_slab,))
    position = jnp.argsort(slab_owner).reshape(tiles_slab // 2, 2)
    tiles = integrals.T.reshape(tiles_slab, TB, kc)
    mine = jnp.take(tiles, position[:, core], axis=0)
    theirs = jnp.take(tiles, position[:, 1 - core], axis=0)
    from_sibling = lax.ppermute(theirs, "c", SWAP)
    own_owners = jnp.stack([mine, from_sibling], axis=2)
    gathered = lax.all_gather(own_owners, "z", axis=1, tiled=True)
    rows = gathered.shape[1]
    half = rows // 2
    by_y = gathered.reshape(ny, nxl, rows, 2, kc)

    amp = jnp.concatenate([amplitudes, lax.ppermute(amplitudes, "xh", SWAP)], axis=1)
    amp = jnp.stack([amp, lax.ppermute(amp, "c", SWAP)], axis=0)

    def block(y_owner, part):
        lhs = lax.dynamic_index_in_dim(by_y, y_owner % ny, 0, keepdims=False)
        lhs = lhs[:, part * half : (part + 1) * half]
        product = lax.dot_general(
            lhs, amp, (((2, 3), (0, 1)), ((), ())), preferred_element_type=jnp.float32
        )
        return lax.optimization_barrier(product)

    to_next = [(i, (i + 1) % ny) for i in range(ny)]
    to_prev = [(i, (i - 1) % ny) for i in range(ny)]
    acc_ahead = block(yi + ny - 1, 0)
    acc_back = block(yi + 1, 1)
    for step in range(ny - 1):
        got_ahead = lax.ppermute(acc_ahead, "y", to_next)
        got_back = lax.ppermute(acc_back, "y", to_prev)
        acc_ahead = got_ahead + block(yi + 2 * ny - 2 - step, 0)
        acc_back = got_back + block(yi + 2 + step, 1)

    kept, came = [], []
    for acc in (acc_ahead, acc_back):
        here = lax.dynamic_index_in_dim(acc, xi, 0, keepdims=False)
        there = lax.dynamic_index_in_dim(acc, 1 - xi, 0, keepdims=False)
        summed = here + lax.ppermute(there, "xl", SWAP)
        kept.append(summed[:, :width])
        came.append(lax.ppermute(summed[:, width:], "xh", SWAP))
    first = jnp.concatenate(kept + came, axis=0)
    second = jnp.concatenate(came + kept, axis=0)
    return jnp.where(xh == 0, first, second)


def solution(mesh):
    n_loop, n_long = mesh.devices.shape
    fine = Mesh(
        mesh.devices.reshape(2, n_loop // 2, n_long // 4, 2, 2), LOOP_AXES + LONG_AXES
    )
    placed = P(LONG_AXES, LOOP_AXES)
    return jax.shard_map(
        local,
        mesh=fine,
        in_specs=(placed, placed, P()),
        out_specs=placed,
        check_vma=False,
    )
```

```python
import jax
import jax.numpy as jnp
from jax import lax
from jax.sharding import Mesh
from jax.sharding import PartitionSpec as P

TB = 50
LOOP_AXES = ("xh", "z")
LONG_AXES = ("y", "xl", "c")
SWAP = [(0, 1), (1, 0)]


def local(amplitudes, integrals, owner):
    nz = lax.axis_size("z")
    ny = lax.axis_size("y")
    nxl = lax.axis_size("xl")
    kc = integrals.shape[0]
    width = amplitudes.shape[1]
    tiles_slab = integrals.shape[1] // TB
    xh = lax.axis_index("xh")
    yi = lax.axis_index("y")
    xi = lax.axis_index("xl")
    core = lax.axis_index("c")
    slab = xh * nz + lax.axis_index("z")

    slab_owner = lax.dynamic_slice(owner, (slab * tiles_slab,), (tiles_slab,))
    position = jnp.argsort(slab_owner).reshape(tiles_slab // 2, 2)
    tiles = integrals.T.reshape(tiles_slab, TB, kc)
    mine = jnp.take(tiles, position[:, core], axis=0)
    theirs = jnp.take(tiles, position[:, 1 - core], axis=0)
    from_sibling = lax.ppermute(theirs, "c", SWAP)
    own_owners = jnp.stack([mine, from_sibling], axis=2)
    gathered = lax.all_gather(own_owners, "z", axis=1, tiled=True)
    rows = gathered.shape[1]
    by_y = gathered.reshape(ny, nxl, rows, 2, kc)

    amp = jnp.concatenate([amplitudes, lax.ppermute(amplitudes, "xh", SWAP)], axis=1)
    amp = jnp.stack([amp, lax.ppermute(amp, "c", SWAP)], axis=0)

    def block(y_owner, low, high):
        lhs = lax.dynamic_index_in_dim(by_y, y_owner % ny, 0, keepdims=False)
        product = lax.dot_general(
            lhs[:, low:high], amp, (((2, 3), (0, 1)), ((), ())),
            preferred_element_type=jnp.float32,
        )
        return lax.optimization_barrier(product)

    to_next = [(i, (i + 1) % ny) for i in range(ny)]
    to_prev = [(i, (i - 1) % ny) for i in range(ny)]

    def ring(first_ahead, first_back, next_ahead, next_back):
        acc_ahead, acc_back = first_ahead, first_back
        for step in range(ny - 1):
            got_ahead = lax.ppermute(acc_ahead, "y", to_next)
            got_back = lax.ppermute(acc_back, "y", to_prev)
            acc_ahead = got_ahead + next_ahead(yi + 2 * ny - 2 - step)
            acc_back = got_back + next_back(yi + 2 + step)
        return acc_ahead, acc_back

    def pair_sum(acc):
        here = lax.dynamic_index_in_dim(acc, xi, 0, keepdims=False)
        there = lax.dynamic_index_in_dim(acc, 1 - xi, 0, keepdims=False)
        return here + lax.ppermute(there, "xl", SWAP)

    y_rows = 8 * (rows * 5 // 72)
    y_half = y_rows // 2
    x_half = 8 * ((rows - y_rows) // 16)
    late = lax.dot_general(
        gathered[:, y_rows:], amp, (((2, 3), (0, 1)), ((), ())),
        preferred_element_type=jnp.float32,
    ).reshape(ny, nxl, rows - y_rows, amp.shape[-1])
    late_here = lax.dynamic_index_in_dim(late, xi, 1, keepdims=False)
    late_there = lax.dynamic_index_in_dim(late, 1 - xi, 1, keepdims=False)
    late_sum = late_here + lax.ppermute(late_there, "xl", SWAP)
    late_ahead, late_back = late_sum[:, :x_half], late_sum[:, x_half:]

    def pick(parts):
        return lambda y_owner: lax.dynamic_index_in_dim(parts, y_owner % ny, 0, keepdims=False)

    early = ring(
        block(yi + ny - 1, 0, y_half),
        block(yi + 1, y_half, y_rows),
        lambda y_owner: block(y_owner, 0, y_half),
        lambda y_owner: block(y_owner, y_half, y_rows),
    )
    late_done = ring(
        pick(late_ahead)(yi + ny - 1),
        pick(late_back)(yi + 1),
        pick(late_ahead),
        pick(late_back),
    )
    pieces = [pair_sum(early[0]), pair_sum(early[1]), late_done[0], late_done[1]]

    kept = [piece[:, :width] for piece in pieces]
    came = [lax.ppermute(piece[:, width:], "xh", SWAP) for piece in pieces]
    first = jnp.concatenate(kept + came, axis=0)
    second = jnp.concatenate(came + kept, axis=0)
    return jnp.where(xh == 0, first, second)


def solution(mesh):
    n_loop, n_long = mesh.devices.shape
    fine = Mesh(
        mesh.devices.reshape(2, n_loop // 2, n_long // 4, 2, 2), LOOP_AXES + LONG_AXES
    )
    placed = P(LONG_AXES, LOOP_AXES)
    return jax.shard_map(
        local,
        mesh=fine,
        in_specs=(placed, placed, P()),
        out_specs=placed,
        check_vma=False,
    )
```

```python
import jax
import jax.numpy as jnp
from jax import lax
from jax.sharding import Mesh
from jax.sharding import PartitionSpec as P

TB = 50
LOOP_AXES = ("xh", "z")
LONG_AXES = ("y", "xl", "c")
SWAP = [(0, 1), (1, 0)]


def local(amplitudes, integrals, owner):
    nz = lax.axis_size("z")
    ny = lax.axis_size("y")
    nxl = lax.axis_size("xl")
    kc = integrals.shape[0]
    width = amplitudes.shape[1]
    tiles_slab = integrals.shape[1] // TB
    xh = lax.axis_index("xh")
    yi = lax.axis_index("y")
    xi = lax.axis_index("xl")
    core = lax.axis_index("c")
    slab = xh * nz + lax.axis_index("z")

    slab_owner = lax.dynamic_slice(owner, (slab * tiles_slab,), (tiles_slab,))
    position = jnp.argsort(slab_owner).reshape(tiles_slab // 2, 2)
    tiles = integrals.T.reshape(tiles_slab, TB, kc)
    mine = jnp.take(tiles, position[:, core], axis=0)
    theirs = jnp.take(tiles, position[:, 1 - core], axis=0)
    from_sibling = lax.ppermute(theirs, "c", SWAP)
    own_owners = jnp.stack([mine, from_sibling], axis=2)
    y_cut = TB * 13 // 25
    gathered = lax.all_gather(own_owners[:, :y_cut], "z", axis=1, tiled=True)
    gathered_late = lax.all_gather(own_owners[:, y_cut:], "z", axis=1, tiled=True)
    y_rows = gathered.shape[1]
    by_y = gathered.reshape(ny, nxl, y_rows, 2, kc)

    amp = jnp.concatenate([amplitudes, lax.ppermute(amplitudes, "xh", SWAP)], axis=1)
    amp = jnp.stack([amp, lax.ppermute(amp, "c", SWAP)], axis=0)

    def block(y_owner, low, high):
        lhs = lax.dynamic_index_in_dim(by_y, y_owner % ny, 0, keepdims=False)
        product = lax.dot_general(
            lhs[:, low:high], amp, (((2, 3), (0, 1)), ((), ())),
            preferred_element_type=jnp.float32,
        )
        return lax.optimization_barrier(product)

    to_next = [(i, (i + 1) % ny) for i in range(ny)]
    to_prev = [(i, (i - 1) % ny) for i in range(ny)]

    def ring(first_ahead, first_back, next_ahead, next_back):
        acc_ahead, acc_back = first_ahead, first_back
        for step in range(ny - 1):
            got_ahead = lax.ppermute(acc_ahead, "y", to_next)
            got_back = lax.ppermute(acc_back, "y", to_prev)
            acc_ahead = got_ahead + next_ahead(yi + 2 * ny - 2 - step)
            acc_back = got_back + next_back(yi + 2 + step)
        return acc_ahead, acc_back

    def pair_sum(acc):
        here = lax.dynamic_index_in_dim(acc, xi, 0, keepdims=False)
        there = lax.dynamic_index_in_dim(acc, 1 - xi, 0, keepdims=False)
        return here + lax.ppermute(there, "xl", SWAP)

    y_half = y_rows // 2
    x_rows = gathered_late.shape[1]
    x_half = 8 * (x_rows // 16)
    late = lax.dot_general(
        gathered_late, amp, (((2, 3), (0, 1)), ((), ())),
        preferred_element_type=jnp.float32,
    ).reshape(ny, nxl, x_rows, amp.shape[-1])
    late_here = lax.dynamic_index_in_dim(late, xi, 1, keepdims=False)
    late_there = lax.dynamic_index_in_dim(late, 1 - xi, 1, keepdims=False)
    late_sum = late_here + lax.ppermute(late_there, "xl", SWAP)
    late_ahead, late_back = late_sum[:, :x_half], late_sum[:, x_half:]

    def pick(parts):
        return lambda y_owner: lax.dynamic_index_in_dim(parts, y_owner % ny, 0, keepdims=False)

    early = ring(
        block(yi + ny - 1, 0, y_half),
        block(yi + 1, y_half, y_rows),
        lambda y_owner: block(y_owner, 0, y_half),
        lambda y_owner: block(y_owner, y_half, y_rows),
    )
    late_done = ring(
        pick(late_ahead)(yi + ny - 1),
        pick(late_back)(yi + 1),
        pick(late_ahead),
        pick(late_back),
    )
    pieces = [pair_sum(early[0]), pair_sum(early[1]), late_done[0], late_done[1]]

    kept = [piece[:, :width] for piece in pieces]
    came = [lax.ppermute(piece[:, width:], "xh", SWAP) for piece in pieces]

    def slab_group(parts):
        early = jnp.concatenate(parts[:2], axis=0).reshape(nz, y_cut, width)
        late_rows = jnp.concatenate(parts[2:], axis=0).reshape(nz, TB - y_cut, width)
        return jnp.concatenate([early, late_rows], axis=1).reshape(nz * TB, width)

    kept, came = slab_group(kept), slab_group(came)
    first = jnp.concatenate([kept, came], axis=0)
    second = jnp.concatenate([came, kept], axis=0)
    return jnp.where(xh == 0, first, second)


def solution(mesh):
    n_loop, n_long = mesh.devices.shape
    fine = Mesh(
        mesh.devices.reshape(2, n_loop // 2, n_long // 4, 2, 2), LOOP_AXES + LONG_AXES
    )
    placed = P(LONG_AXES, LOOP_AXES)
    return jax.shard_map(
        local,
        mesh=fine,
        in_specs=(placed, placed, P()),
        out_specs=placed,
        check_vma=False,
    )
```

```python
import jax
import jax.numpy as jnp
from jax import lax
from jax.sharding import Mesh
from jax.sharding import PartitionSpec as P

TB = 50
LOOP_AXES = ("xh", "z")
LONG_AXES = ("y", "xl", "c")
SWAP = [(0, 1), (1, 0)]


def local(amplitudes, integrals, owner):
    nz = lax.axis_size("z")
    ny = lax.axis_size("y")
    nxl = lax.axis_size("xl")
    kc = integrals.shape[0]
    width = amplitudes.shape[1]
    tiles_slab = integrals.shape[1] // TB
    xh = lax.axis_index("xh")
    yi = lax.axis_index("y")
    xi = lax.axis_index("xl")
    core = lax.axis_index("c")
    slab = xh * nz + lax.axis_index("z")

    slab_owner = lax.dynamic_slice(owner, (slab * tiles_slab,), (tiles_slab,))
    position = jnp.argsort(slab_owner).reshape(tiles_slab // 2, 2)
    tiles = integrals.T.reshape(tiles_slab, TB, kc)
    mine = jnp.take(tiles, position[:, core], axis=0)
    theirs = jnp.take(tiles, position[:, 1 - core], axis=0)
    from_sibling = lax.ppermute(theirs, "c", SWAP)
    own_owners = jnp.stack([mine, from_sibling], axis=2)
    y_cut = TB * 3 // 5
    gathered = lax.all_gather(own_owners[:, :y_cut], "z", axis=1, tiled=True)
    gathered_late = lax.all_gather(own_owners[:, y_cut:], "z", axis=1, tiled=True)
    y_rows = gathered.shape[1]
    by_y = gathered.reshape(ny, nxl, y_rows, 2, kc)

    amp = jnp.concatenate([amplitudes, lax.ppermute(amplitudes, "xh", SWAP)], axis=1)
    amp = jnp.stack([amp, lax.ppermute(amp, "c", SWAP)], axis=0)

    def block(y_owner, low, high):
        lhs = lax.dynamic_index_in_dim(by_y, y_owner % ny, 0, keepdims=False)
        product = lax.dot_general(
            lhs[:, low:high], amp, (((2, 3), (0, 1)), ((), ())),
            preferred_element_type=jnp.float32,
        )
        return lax.optimization_barrier(product)

    to_next = [(i, (i + 1) % ny) for i in range(ny)]
    to_prev = [(i, (i - 1) % ny) for i in range(ny)]

    def ring(first_ahead, first_back, next_ahead, next_back):
        acc_ahead, acc_back = first_ahead, first_back
        for step in range(ny - 1):
            got_ahead = lax.ppermute(acc_ahead, "y", to_next)
            got_back = lax.ppermute(acc_back, "y", to_prev)
            acc_ahead = got_ahead + next_ahead(yi + 2 * ny - 2 - step)
            acc_back = got_back + next_back(yi + 2 + step)
        return acc_ahead, acc_back

    def pair_sum(acc):
        here = lax.dynamic_index_in_dim(acc, xi, 0, keepdims=False)
        there = lax.dynamic_index_in_dim(acc, 1 - xi, 0, keepdims=False)
        return here + lax.ppermute(there, "xl", SWAP)

    y_half = y_rows // 2
    x_rows = gathered_late.shape[1]
    x_half = 8 * (x_rows // 16)
    late = lax.dot_general(
        gathered_late, amp, (((2, 3), (0, 1)), ((), ())),
        preferred_element_type=jnp.float32,
    ).reshape(ny, nxl, x_rows, amp.shape[-1])
    late_here = lax.dynamic_index_in_dim(late, xi, 1, keepdims=False)
    late_there = lax.dynamic_index_in_dim(late, 1 - xi, 1, keepdims=False)
    late_sum = late_here + lax.ppermute(late_there, "xl", SWAP)
    late_ahead, late_back = late_sum[:, :x_half], late_sum[:, x_half:]

    def pick(parts):
        return lambda y_owner: lax.dynamic_index_in_dim(parts, y_owner % ny, 0, keepdims=False)

    early = ring(
        block(yi + ny - 1, 0, y_half),
        block(yi + 1, y_half, y_rows),
        lambda y_owner: block(y_owner, 0, y_half),
        lambda y_owner: block(y_owner, y_half, y_rows),
    )
    late_done = ring(
        pick(late_ahead)(yi + ny - 1),
        pick(late_back)(yi + 1),
        pick(late_ahead),
        pick(late_back),
    )
    pieces = [pair_sum(early[0]), pair_sum(early[1]), late_done[0], late_done[1]]

    kept = [piece[:, :width] for piece in pieces]
    came = [lax.ppermute(piece[:, width:], "xh", SWAP) for piece in pieces]

    def slab_group(parts):
        early = jnp.concatenate(parts[:2], axis=0).reshape(nz, y_cut, width)
        late_rows = jnp.concatenate(parts[2:], axis=0).reshape(nz, TB - y_cut, width)
        return jnp.concatenate([early, late_rows], axis=1).reshape(nz * TB, width)

    kept, came = slab_group(kept), slab_group(came)
    first = jnp.concatenate([kept, came], axis=0)
    second = jnp.concatenate([came, kept], axis=0)
    return jnp.where(xh == 0, first, second)


def solution(mesh):
    n_loop, n_long = mesh.devices.shape
    fine = Mesh(
        mesh.devices.reshape(2, n_loop // 2, n_long // 4, 2, 2), LOOP_AXES + LONG_AXES
    )
    placed = P(LONG_AXES, LOOP_AXES)
    return jax.shard_map(
        local,
        mesh=fine,
        in_specs=(placed, placed, P()),
        out_specs=placed,
        check_vma=False,
    )
```

```python
import jax
import jax.numpy as jnp
from jax import lax
from jax.sharding import Mesh
from jax.sharding import PartitionSpec as P

TB = 50
LOOP_AXES = ("xh", "z")
LONG_AXES = ("y", "xl", "c")
SWAP = [(0, 1), (1, 0)]


def local(amplitudes, integrals, owner):
    nz = lax.axis_size("z")
    ny = lax.axis_size("y")
    nxl = lax.axis_size("xl")
    kc = integrals.shape[0]
    width = amplitudes.shape[1]
    tiles_slab = integrals.shape[1] // TB
    xh = lax.axis_index("xh")
    yi = lax.axis_index("y")
    xi = lax.axis_index("xl")
    core = lax.axis_index("c")
    slab = xh * nz + lax.axis_index("z")

    slab_owner = lax.dynamic_slice(owner, (slab * tiles_slab,), (tiles_slab,))
    position = jnp.argsort(slab_owner).reshape(tiles_slab // 2, 2)
    tiles = integrals.T.reshape(tiles_slab, TB, kc)
    mine = jnp.take(tiles, position[:, core], axis=0)
    theirs = jnp.take(tiles, position[:, 1 - core], axis=0)
    from_sibling = lax.ppermute(theirs, "c", SWAP)
    own_owners = jnp.stack([mine, from_sibling], axis=2)
    y_cut = TB * 3 // 5
    gathered = lax.all_gather(own_owners[:, :y_cut], "z", axis=1, tiled=True)
    late_rows, gathered = lax.optimization_barrier((own_owners[:, y_cut:], gathered))
    gathered_late = lax.all_gather(late_rows, "z", axis=1, tiled=True)
    y_rows = gathered.shape[1]
    by_y = gathered.reshape(ny, nxl, y_rows, 2, kc)

    amp = jnp.concatenate([amplitudes, lax.ppermute(amplitudes, "xh", SWAP)], axis=1)
    amp = jnp.stack([amp, lax.ppermute(amp, "c", SWAP)], axis=0)

    def block(y_owner, low, high):
        lhs = lax.dynamic_index_in_dim(by_y, y_owner % ny, 0, keepdims=False)
        product = lax.dot_general(
            lhs[:, low:high], amp, (((2, 3), (0, 1)), ((), ())),
            preferred_element_type=jnp.float32,
        )
        return lax.optimization_barrier(product)

    to_next = [(i, (i + 1) % ny) for i in range(ny)]
    to_prev = [(i, (i - 1) % ny) for i in range(ny)]

    def ring(first_ahead, first_back, next_ahead, next_back):
        acc_ahead, acc_back = first_ahead, first_back
        for step in range(ny - 1):
            got_ahead = lax.ppermute(acc_ahead, "y", to_next)
            got_back = lax.ppermute(acc_back, "y", to_prev)
            acc_ahead = got_ahead + next_ahead(yi + 2 * ny - 2 - step)
            acc_back = got_back + next_back(yi + 2 + step)
        return acc_ahead, acc_back

    def pair_sum(acc):
        here = lax.dynamic_index_in_dim(acc, xi, 0, keepdims=False)
        there = lax.dynamic_index_in_dim(acc, 1 - xi, 0, keepdims=False)
        return here + lax.ppermute(there, "xl", SWAP)

    y_half = y_rows // 2
    x_rows = gathered_late.shape[1]
    x_half = 8 * (x_rows // 16)
    late = lax.dot_general(
        gathered_late, amp, (((2, 3), (0, 1)), ((), ())),
        preferred_element_type=jnp.float32,
    ).reshape(ny, nxl, x_rows, amp.shape[-1])
    late_here = lax.dynamic_index_in_dim(late, xi, 1, keepdims=False)
    late_there = lax.dynamic_index_in_dim(late, 1 - xi, 1, keepdims=False)
    late_sum = late_here + lax.ppermute(late_there, "xl", SWAP)
    late_ahead, late_back = late_sum[:, :x_half], late_sum[:, x_half:]

    def pick(parts):
        return lambda y_owner: lax.dynamic_index_in_dim(parts, y_owner % ny, 0, keepdims=False)

    early = ring(
        block(yi + ny - 1, 0, y_half),
        block(yi + 1, y_half, y_rows),
        lambda y_owner: block(y_owner, 0, y_half),
        lambda y_owner: block(y_owner, y_half, y_rows),
    )
    late_done = ring(
        pick(late_ahead)(yi + ny - 1),
        pick(late_back)(yi + 1),
        pick(late_ahead),
        pick(late_back),
    )
    pieces = [pair_sum(early[0]), pair_sum(early[1]), late_done[0], late_done[1]]

    kept = [piece[:, :width] for piece in pieces]
    came = [lax.ppermute(piece[:, width:], "xh", SWAP) for piece in pieces]

    def slab_group(parts):
        early = jnp.concatenate(parts[:2], axis=0).reshape(nz, y_cut, width)
        late_rows = jnp.concatenate(parts[2:], axis=0).reshape(nz, TB - y_cut, width)
        return jnp.concatenate([early, late_rows], axis=1).reshape(nz * TB, width)

    kept, came = slab_group(kept), slab_group(came)
    first = jnp.concatenate([kept, came], axis=0)
    second = jnp.concatenate([came, kept], axis=0)
    return jnp.where(xh == 0, first, second)


def solution(mesh):
    n_loop, n_long = mesh.devices.shape
    fine = Mesh(
        mesh.devices.reshape(2, n_loop // 2, n_long // 4, 2, 2), LOOP_AXES + LONG_AXES
    )
    placed = P(LONG_AXES, LOOP_AXES)
    return jax.shard_map(
        local,
        mesh=fine,
        in_specs=(placed, placed, P()),
        out_specs=placed,
        check_vma=False,
    )
```

```python
import jax
import jax.numpy as jnp
from jax import lax
from jax.sharding import Mesh
from jax.sharding import PartitionSpec as P

TB = 50
LOOP_AXES = ("xh", "z")
LONG_AXES = ("y", "xl", "c")
SWAP = [(0, 1), (1, 0)]


def local(amplitudes, integrals, owner):
    nz = lax.axis_size("z")
    ny = lax.axis_size("y")
    nxl = lax.axis_size("xl")
    kc = integrals.shape[0]
    width = amplitudes.shape[1]
    tiles_slab = integrals.shape[1] // TB
    xh = lax.axis_index("xh")
    yi = lax.axis_index("y")
    xi = lax.axis_index("xl")
    core = lax.axis_index("c")
    slab = xh * nz + lax.axis_index("z")

    slab_owner = lax.dynamic_slice(owner, (slab * tiles_slab,), (tiles_slab,))
    position = jnp.argsort(slab_owner).reshape(tiles_slab // 2, 2)
    tiles = integrals.T.reshape(tiles_slab, TB, kc)
    mine = jnp.take(tiles, position[:, core], axis=0)
    theirs = jnp.take(tiles, position[:, 1 - core], axis=0)
    from_sibling = lax.ppermute(theirs, "c", SWAP)
    own_owners = jnp.stack([mine, from_sibling], axis=2)
    y_cut = TB * 14 // 25
    gathered = lax.all_gather(own_owners[:, :y_cut], "z", axis=1, tiled=True)
    y_rows = gathered.shape[1]
    by_y = gathered.reshape(ny, nxl, y_rows, 2, kc)

    amp = jnp.concatenate([amplitudes, lax.ppermute(amplitudes, "xh", SWAP)], axis=1)
    late_rows, amp = lax.optimization_barrier((own_owners[:, y_cut:], amp))
    gathered_late = lax.all_gather(late_rows, "z", axis=1, tiled=True)
    amp = jnp.stack([amp, lax.ppermute(amp, "c", SWAP)], axis=0)

    def block(y_owner, low, high):
        lhs = lax.dynamic_index_in_dim(by_y, y_owner % ny, 0, keepdims=False)
        product = lax.dot_general(
            lhs[:, low:high], amp, (((2, 3), (0, 1)), ((), ())),
            preferred_element_type=jnp.float32,
        )
        return lax.optimization_barrier(product)

    to_next = [(i, (i + 1) % ny) for i in range(ny)]
    to_prev = [(i, (i - 1) % ny) for i in range(ny)]

    def ring(first_ahead, first_back, next_ahead, next_back):
        acc_ahead, acc_back = first_ahead, first_back
        for step in range(ny - 1):
            got_ahead = lax.ppermute(acc_ahead, "y", to_next)
            got_back = lax.ppermute(acc_back, "y", to_prev)
            acc_ahead = got_ahead + next_ahead(yi + 2 * ny - 2 - step)
            acc_back = got_back + next_back(yi + 2 + step)
        return acc_ahead, acc_back

    def pair_sum(acc):
        here = lax.dynamic_index_in_dim(acc, xi, 0, keepdims=False)
        there = lax.dynamic_index_in_dim(acc, 1 - xi, 0, keepdims=False)
        return here + lax.ppermute(there, "xl", SWAP)

    y_half = y_rows // 2
    x_rows = gathered_late.shape[1]
    x_half = 8 * (x_rows // 16)
    late_by_xl = gathered_late.reshape(ny, nxl, x_rows, 2, kc)

    def late_block(x_owner):
        lhs = lax.dynamic_index_in_dim(late_by_xl, x_owner, 1, keepdims=False)
        product = lax.dot_general(
            lhs, amp, (((2, 3), (0, 1)), ((), ())), preferred_element_type=jnp.float32
        )
        return lax.optimization_barrier(product)

    late_there = late_block(1 - xi)
    late_sum = late_block(xi) + lax.ppermute(late_there, "xl", SWAP)
    late_ahead, late_back = late_sum[:, :x_half], late_sum[:, x_half:]

    def pick(parts):
        return lambda y_owner: lax.dynamic_index_in_dim(parts, y_owner % ny, 0, keepdims=False)

    early = ring(
        block(yi + ny - 1, 0, y_half),
        block(yi + 1, y_half, y_rows),
        lambda y_owner: block(y_owner, 0, y_half),
        lambda y_owner: block(y_owner, y_half, y_rows),
    )
    late_done = ring(
        pick(late_ahead)(yi + ny - 1),
        pick(late_back)(yi + 1),
        pick(late_ahead),
        pick(late_back),
    )
    pieces = [pair_sum(early[0]), pair_sum(early[1]), late_done[0], late_done[1]]

    kept = [piece[:, :width] for piece in pieces]
    came = [lax.ppermute(piece[:, width:], "xh", SWAP) for piece in pieces]

    def slab_group(parts):
        early = jnp.concatenate(parts[:2], axis=0).reshape(nz, y_cut, width)
        late_rows = jnp.concatenate(parts[2:], axis=0).reshape(nz, TB - y_cut, width)
        return jnp.concatenate([early, late_rows], axis=1).reshape(nz * TB, width)

    kept, came = slab_group(kept), slab_group(came)
    first = jnp.concatenate([kept, came], axis=0)
    second = jnp.concatenate([came, kept], axis=0)
    return jnp.where(xh == 0, first, second)


def solution(mesh):
    n_loop, n_long = mesh.devices.shape
    fine = Mesh(
        mesh.devices.reshape(2, n_loop // 2, n_long // 4, 2, 2), LOOP_AXES + LONG_AXES
    )
    placed = P(LONG_AXES, LOOP_AXES)
    return jax.shard_map(
        local,
        mesh=fine,
        in_specs=(placed, placed, P()),
        out_specs=placed,
        check_vma=False,
    )
```

```python
import jax
import jax.numpy as jnp
from jax import lax
from jax.sharding import Mesh
from jax.sharding import PartitionSpec as P

TB = 50
LOOP_AXES = ("xh", "z")
LONG_AXES = ("y", "xl", "c")
SWAP = [(0, 1), (1, 0)]


def local(amplitudes, integrals, owner):
    nz = lax.axis_size("z")
    ny = lax.axis_size("y")
    nxl = lax.axis_size("xl")
    kc = integrals.shape[0]
    width = amplitudes.shape[1]
    tiles_slab = integrals.shape[1] // TB
    xh = lax.axis_index("xh")
    yi = lax.axis_index("y")
    xi = lax.axis_index("xl")
    core = lax.axis_index("c")
    slab = xh * nz + lax.axis_index("z")

    slab_owner = lax.dynamic_slice(owner, (slab * tiles_slab,), (tiles_slab,))
    position = jnp.argsort(slab_owner).reshape(tiles_slab // 2, 2)
    tiles = integrals.T.reshape(tiles_slab, TB, kc)
    mine = jnp.take(tiles, position[:, core], axis=0)
    theirs = jnp.take(tiles, position[:, 1 - core], axis=0)
    from_sibling = lax.ppermute(theirs, "c", SWAP)
    own_owners = jnp.stack([mine, from_sibling], axis=2)
    y_cut = TB * 14 // 25
    gathered = lax.all_gather(own_owners[:, :y_cut], "z", axis=1, tiled=True)
    y_rows = gathered.shape[1]
    by_y = gathered.reshape(ny, nxl, y_rows, 2, kc)

    amp = jnp.concatenate([amplitudes, lax.ppermute(amplitudes, "xh", SWAP)], axis=1)
    late_rows, amp = lax.optimization_barrier((own_owners[:, y_cut:], amp))
    gathered_late = lax.all_gather(late_rows, "z", axis=1, tiled=True)
    amp = jnp.stack([amp, lax.ppermute(amp, "c", SWAP)], axis=0)

    def block(y_owner, low, high):
        lhs = lax.dynamic_index_in_dim(by_y, y_owner % ny, 0, keepdims=False)
        product = lax.dot_general(
            lhs[:, low:high], amp, (((2, 3), (0, 1)), ((), ())),
            preferred_element_type=jnp.float32,
        )
        return lax.optimization_barrier(product)

    to_next = [(i, (i + 1) % ny) for i in range(ny)]
    to_prev = [(i, (i - 1) % ny) for i in range(ny)]

    def ring(first_ahead, first_back, next_ahead, next_back):
        acc_ahead, acc_back = first_ahead, first_back
        for step in range(ny - 1):
            got_ahead = lax.ppermute(acc_ahead, "y", to_next)
            got_back = lax.ppermute(acc_back, "y", to_prev)
            acc_ahead = got_ahead + next_ahead(yi + 2 * ny - 2 - step)
            acc_back = got_back + next_back(yi + 2 + step)
        return acc_ahead, acc_back

    def pair_sum(acc):
        here = lax.dynamic_index_in_dim(acc, xi, 0, keepdims=False)
        there = lax.dynamic_index_in_dim(acc, 1 - xi, 0, keepdims=False)
        return here + lax.ppermute(there, "xl", SWAP)

    y_half = y_rows // 2
    x_rows = gathered_late.shape[1]
    late_by_xl = gathered_late.reshape(ny, nxl, x_rows, 2, kc)

    def late_block(x_owner):
        lhs = lax.dynamic_index_in_dim(late_by_xl, x_owner, 1, keepdims=False)
        product = lax.dot_general(
            lhs, amp, (((2, 3), (0, 1)), ((), ())), preferred_element_type=jnp.float32
        )
        return lax.optimization_barrier(product)

    late_there = late_block(1 - xi)
    late_sum = late_block(xi) + lax.ppermute(late_there, "xl", SWAP)

    def pick(parts):
        return lambda y_owner: lax.dynamic_index_in_dim(parts, y_owner % ny, 0, keepdims=False)

    early = ring(
        block(yi + ny - 1, 0, y_half),
        block(yi + 1, y_half, y_rows),
        lambda y_owner: block(y_owner, 0, y_half),
        lambda y_owner: block(y_owner, y_half, y_rows),
    )
    late_done = pick(late_sum)(yi)
    for hop in range(1, ny):
        to_owner = [(i, (i + hop) % ny) for i in range(ny)]
        late_done = late_done + lax.ppermute(pick(late_sum)(yi + hop), "y", to_owner)
    pieces = [pair_sum(early[0]), pair_sum(early[1]), late_done]

    kept = [piece[:, :width] for piece in pieces]
    came = [lax.ppermute(piece[:, width:], "xh", SWAP) for piece in pieces]

    def slab_group(parts):
        early = jnp.concatenate(parts[:2], axis=0).reshape(nz, y_cut, width)
        late_rows = jnp.concatenate(parts[2:], axis=0).reshape(nz, TB - y_cut, width)
        return jnp.concatenate([early, late_rows], axis=1).reshape(nz * TB, width)

    kept, came = slab_group(kept), slab_group(came)
    first = jnp.concatenate([kept, came], axis=0)
    second = jnp.concatenate([came, kept], axis=0)
    return jnp.where(xh == 0, first, second)


def solution(mesh):
    n_loop, n_long = mesh.devices.shape
    fine = Mesh(
        mesh.devices.reshape(2, n_loop // 2, n_long // 4, 2, 2), LOOP_AXES + LONG_AXES
    )
    placed = P(LONG_AXES, LOOP_AXES)
    return jax.shard_map(
        local,
        mesh=fine,
        in_specs=(placed, placed, P()),
        out_specs=placed,
        check_vma=False,
    )
```

```python
import jax
import jax.numpy as jnp
from jax import lax
from jax.sharding import Mesh
from jax.sharding import PartitionSpec as P

TB = 50
LOOP_AXES = ("xh", "z")
LONG_AXES = ("y", "xl", "c")
SWAP = [(0, 1), (1, 0)]


def local(amplitudes, integrals, owner):
    nz = lax.axis_size("z")
    ny = lax.axis_size("y")
    nxl = lax.axis_size("xl")
    kc = integrals.shape[0]
    width = amplitudes.shape[1]
    tiles_slab = integrals.shape[1] // TB
    xh = lax.axis_index("xh")
    yi = lax.axis_index("y")
    xi = lax.axis_index("xl")
    core = lax.axis_index("c")
    slab = xh * nz + lax.axis_index("z")

    slab_owner = lax.dynamic_slice(owner, (slab * tiles_slab,), (tiles_slab,))
    position = jnp.argsort(slab_owner).reshape(tiles_slab // 2, 2)
    tiles = integrals.T.reshape(tiles_slab, TB, kc)
    mine = jnp.take(tiles, position[:, core], axis=0)
    theirs = jnp.take(tiles, position[:, 1 - core], axis=0)
    from_sibling = lax.ppermute(theirs, "c", SWAP)
    own_owners = jnp.stack([mine, from_sibling], axis=2)
    y_cut = TB * 14 // 25
    gathered = lax.all_gather(own_owners[:, :y_cut], "z", axis=1, tiled=True)
    y_rows = gathered.shape[1]
    by_y = gathered.reshape(ny, nxl, y_rows, 2, kc)

    amp = jnp.concatenate([amplitudes, lax.ppermute(amplitudes, "xh", SWAP)], axis=1)
    late_rows, amp = lax.optimization_barrier((own_owners[:, y_cut:], amp))
    gathered_late = lax.all_gather(late_rows, "z", axis=1, tiled=True)
    amp = jnp.stack([amp, lax.ppermute(amp, "c", SWAP)], axis=0)

    def block(y_owner, low, high):
        lhs = lax.dynamic_index_in_dim(by_y, y_owner % ny, 0, keepdims=False)
        product = lax.dot_general(
            lhs[:, low:high], amp, (((2, 3), (0, 1)), ((), ())),
            preferred_element_type=jnp.float32,
        )
        return lax.optimization_barrier(product)

    to_next = [(i, (i + 1) % ny) for i in range(ny)]
    to_prev = [(i, (i - 1) % ny) for i in range(ny)]

    def ring(first_ahead, first_back, next_ahead, next_back):
        acc_ahead, acc_back = first_ahead, first_back
        for step in range(ny - 1):
            got_ahead = lax.ppermute(acc_ahead, "y", to_next)
            got_back = lax.ppermute(acc_back, "y", to_prev)
            acc_ahead = got_ahead + next_ahead(yi + 2 * ny - 2 - step)
            acc_back = got_back + next_back(yi + 2 + step)
        return acc_ahead, acc_back

    def pair_sum(acc):
        here = lax.dynamic_index_in_dim(acc, xi, 0, keepdims=False)
        there = lax.dynamic_index_in_dim(acc, 1 - xi, 0, keepdims=False)
        return here + lax.ppermute(there, "xl", SWAP)

    y_half = y_rows // 2
    x_rows = gathered_late.shape[1]
    late_by_xl = gathered_late.reshape(ny, nxl, x_rows, 2, kc)

    def late_block(x_owner):
        lhs = lax.dynamic_index_in_dim(late_by_xl, x_owner, 1, keepdims=False)
        product = lax.dot_general(
            lhs, amp, (((2, 3), (0, 1)), ((), ())), preferred_element_type=jnp.float32
        )
        return lax.optimization_barrier(product)

    late_there = late_block(1 - xi)
    late_sum = late_block(xi) + lax.ppermute(late_there, "xl", SWAP)

    def pick(parts):
        return lambda y_owner: lax.dynamic_index_in_dim(parts, y_owner % ny, 0, keepdims=False)

    early = block(yi, 0, y_rows)
    for hop in range(1, ny):
        to_owner = [(i, (i + hop) % ny) for i in range(ny)]
        early = early + lax.ppermute(block(yi + hop, 0, y_rows), "y", to_owner)
    late_done = pick(late_sum)(yi)
    for hop in range(1, ny):
        to_owner = [(i, (i + hop) % ny) for i in range(ny)]
        late_done = late_done + lax.ppermute(pick(late_sum)(yi + hop), "y", to_owner)
    pieces = [pair_sum(early), late_done]

    kept = [piece[:, :width] for piece in pieces]
    came = [lax.ppermute(piece[:, width:], "xh", SWAP) for piece in pieces]

    def slab_group(parts):
        early = parts[0].reshape(nz, y_cut, width)
        late_rows = parts[1].reshape(nz, TB - y_cut, width)
        return jnp.concatenate([early, late_rows], axis=1).reshape(nz * TB, width)

    kept, came = slab_group(kept), slab_group(came)
    first = jnp.concatenate([kept, came], axis=0)
    second = jnp.concatenate([came, kept], axis=0)
    return jnp.where(xh == 0, first, second)


def solution(mesh):
    n_loop, n_long = mesh.devices.shape
    fine = Mesh(
        mesh.devices.reshape(2, n_loop // 2, n_long // 4, 2, 2), LOOP_AXES + LONG_AXES
    )
    placed = P(LONG_AXES, LOOP_AXES)
    return jax.shard_map(
        local,
        mesh=fine,
        in_specs=(placed, placed, P()),
        out_specs=placed,
        check_vma=False,
    )
```

```python
import jax
import jax.numpy as jnp
from jax import lax
from jax.sharding import Mesh
from jax.sharding import PartitionSpec as P

TB = 50
LOOP_AXES = ("xh", "z")
LONG_AXES = ("y", "xl", "c")
SWAP = [(0, 1), (1, 0)]


def local(amplitudes, integrals, owner):
    nz = lax.axis_size("z")
    ny = lax.axis_size("y")
    nxl = lax.axis_size("xl")
    kc = integrals.shape[0]
    width = amplitudes.shape[1]
    tiles_slab = integrals.shape[1] // TB
    xh = lax.axis_index("xh")
    yi = lax.axis_index("y")
    xi = lax.axis_index("xl")
    core = lax.axis_index("c")
    slab = xh * nz + lax.axis_index("z")

    slab_owner = lax.dynamic_slice(owner, (slab * tiles_slab,), (tiles_slab,))
    position = jnp.argsort(slab_owner).reshape(tiles_slab // 2, 2)
    tiles = integrals.T.reshape(tiles_slab, TB, kc)
    mine = jnp.take(tiles, position[:, core], axis=0)
    theirs = jnp.take(tiles, position[:, 1 - core], axis=0)
    from_sibling = lax.ppermute(theirs, "c", SWAP)
    own_owners = jnp.stack([mine, from_sibling], axis=2)
    y_cut = TB * 29 // 50
    gathered = lax.all_gather(own_owners[:, :y_cut], "z", axis=1, tiled=True)
    y_rows = gathered.shape[1]
    by_y = gathered.reshape(ny, nxl, y_rows, 2, kc)

    amp = jnp.concatenate([amplitudes, lax.ppermute(amplitudes, "xh", SWAP)], axis=1)
    amp = jnp.stack([amp, lax.ppermute(amp, "c", SWAP)], axis=0)
    late_rows, amp = lax.optimization_barrier((own_owners[:, y_cut:], amp))
    gathered_late = lax.all_gather(late_rows, "z", axis=1, tiled=True)

    def block(y_owner, low, high):
        lhs = lax.dynamic_index_in_dim(by_y, y_owner % ny, 0, keepdims=False)
        product = lax.dot_general(
            lhs[:, low:high], amp, (((2, 3), (0, 1)), ((), ())),
            preferred_element_type=jnp.float32,
        )
        return lax.optimization_barrier(product)

    to_next = [(i, (i + 1) % ny) for i in range(ny)]
    to_prev = [(i, (i - 1) % ny) for i in range(ny)]

    def ring(first_ahead, first_back, next_ahead, next_back):
        acc_ahead, acc_back = first_ahead, first_back
        for step in range(ny - 1):
            got_ahead = lax.ppermute(acc_ahead, "y", to_next)
            got_back = lax.ppermute(acc_back, "y", to_prev)
            acc_ahead = got_ahead + next_ahead(yi + 2 * ny - 2 - step)
            acc_back = got_back + next_back(yi + 2 + step)
        return acc_ahead, acc_back

    def pair_sum(acc):
        here = lax.dynamic_index_in_dim(acc, xi, 0, keepdims=False)
        there = lax.dynamic_index_in_dim(acc, 1 - xi, 0, keepdims=False)
        return here + lax.ppermute(there, "xl", SWAP)

    y_half = y_rows // 2
    x_rows = gathered_late.shape[1]
    late_by_xl = gathered_late.reshape(ny, nxl, x_rows, 2, kc)

    def late_block(x_owner):
        lhs = lax.dynamic_index_in_dim(late_by_xl, x_owner, 1, keepdims=False)
        product = lax.dot_general(
            lhs, amp, (((2, 3), (0, 1)), ((), ())), preferred_element_type=jnp.float32
        )
        return lax.optimization_barrier(product)

    late_there = late_block(1 - xi)
    late_sum = late_block(xi) + lax.ppermute(late_there, "xl", SWAP)

    def pick(parts):
        return lambda y_owner: lax.dynamic_index_in_dim(parts, y_owner % ny, 0, keepdims=False)

    early = ring(
        block(yi + ny - 1, 0, y_half),
        block(yi + 1, y_half, y_rows),
        lambda y_owner: block(y_owner, 0, y_half),
        lambda y_owner: block(y_owner, y_half, y_rows),
    )
    late_done = pick(late_sum)(yi)
    for hop in range(1, ny):
        to_owner = [(i, (i + hop) % ny) for i in range(ny)]
        late_done = late_done + lax.ppermute(pick(late_sum)(yi + hop), "y", to_owner)
    pieces = [pair_sum(early[0]), pair_sum(early[1]), late_done]

    kept = [piece[:, :width] for piece in pieces]
    came = [lax.ppermute(piece[:, width:], "xh", SWAP) for piece in pieces]

    def slab_group(parts):
        early = jnp.concatenate(parts[:2], axis=0).reshape(nz, y_cut, width)
        late_rows = jnp.concatenate(parts[2:], axis=0).reshape(nz, TB - y_cut, width)
        return jnp.concatenate([early, late_rows], axis=1).reshape(nz * TB, width)

    kept, came = slab_group(kept), slab_group(came)
    first = jnp.concatenate([kept, came], axis=0)
    second = jnp.concatenate([came, kept], axis=0)
    return jnp.where(xh == 0, first, second)


def solution(mesh):
    n_loop, n_long = mesh.devices.shape
    fine = Mesh(
        mesh.devices.reshape(2, n_loop // 2, n_long // 4, 2, 2), LOOP_AXES + LONG_AXES
    )
    placed = P(LONG_AXES, LOOP_AXES)
    return jax.shard_map(
        local,
        mesh=fine,
        in_specs=(placed, placed, P()),
        out_specs=placed,
        check_vma=False,
    )
```

```python
import jax
import jax.numpy as jnp
from jax import lax
from jax.sharding import Mesh
from jax.sharding import PartitionSpec as P

TB = 50
LOOP_AXES = ("xh", "z")
LONG_AXES = ("y", "xl", "c")
SWAP = [(0, 1), (1, 0)]


def local(amplitudes, integrals, owner):
    nz = lax.axis_size("z")
    ny = lax.axis_size("y")
    nxl = lax.axis_size("xl")
    kc = integrals.shape[0]
    width = amplitudes.shape[1]
    tiles_slab = integrals.shape[1] // TB
    xh = lax.axis_index("xh")
    yi = lax.axis_index("y")
    xi = lax.axis_index("xl")
    core = lax.axis_index("c")
    slab = xh * nz + lax.axis_index("z")

    slab_owner = lax.dynamic_slice(owner, (slab * tiles_slab,), (tiles_slab,))
    position = jnp.argsort(slab_owner).reshape(tiles_slab // 2, 2)
    tiles = integrals.T.reshape(tiles_slab, TB, kc)
    mine = jnp.take(tiles, position[:, core], axis=0)
    theirs = jnp.take(tiles, position[:, 1 - core], axis=0)
    from_sibling = lax.ppermute(theirs, "c", SWAP)
    own_owners = jnp.stack([mine, from_sibling], axis=2)
    y_cut = TB * 14 // 25
    gathered = lax.all_gather(own_owners[:, :y_cut], "z", axis=1, tiled=True)
    y_rows = gathered.shape[1]
    by_y = gathered.reshape(ny, nxl, y_rows, 2, kc)

    amp = jnp.concatenate([amplitudes, lax.ppermute(amplitudes, "xh", SWAP)], axis=1)
    late_rows, amp = lax.optimization_barrier((own_owners[:, y_cut:], amp))
    gathered_late = lax.all_gather(late_rows, "z", axis=1, tiled=True)
    amp = jnp.stack([amp, lax.ppermute(amp, "c", SWAP)], axis=0)

    def block(y_owner, low, high):
        lhs = lax.dynamic_index_in_dim(by_y, y_owner % ny, 0, keepdims=False)
        product = lax.dot_general(
            lhs[:, low:high], amp, (((2, 3), (0, 1)), ((), ())),
            preferred_element_type=jnp.float32,
        )
        return lax.optimization_barrier(product)

    to_next = [(i, (i + 1) % ny) for i in range(ny)]
    to_prev = [(i, (i - 1) % ny) for i in range(ny)]

    def ring(first_ahead, first_back, next_ahead, next_back):
        acc_ahead, acc_back = first_ahead, first_back
        for step in range(ny - 1):
            got_ahead = lax.ppermute(acc_ahead, "y", to_next)
            got_back = lax.ppermute(acc_back, "y", to_prev)
            acc_ahead = got_ahead + next_ahead(yi + 2 * ny - 2 - step)
            acc_back = got_back + next_back(yi + 2 + step)
        return acc_ahead, acc_back

    def pair_sum(acc):
        here = lax.dynamic_index_in_dim(acc, xi, 0, keepdims=False)
        there = lax.dynamic_index_in_dim(acc, 1 - xi, 0, keepdims=False)
        return here + lax.ppermute(there, "xl", SWAP)

    y_half = y_rows // 2
    x_rows = gathered_late.shape[1]
    late_by_xl = gathered_late.reshape(ny, nxl, x_rows, 2, kc)

    def late_block(x_owner):
        lhs = lax.dynamic_index_in_dim(late_by_xl, x_owner, 1, keepdims=False)
        product = lax.dot_general(
            lhs, amp, (((2, 3), (0, 1)), ((), ())), preferred_element_type=jnp.float32
        )
        return lax.optimization_barrier(product)

    late_there = late_block(1 - xi)
    late_sum = late_block(xi) + lax.ppermute(late_there, "xl", SWAP)

    def pick(parts):
        return lambda y_owner: lax.dynamic_index_in_dim(parts, y_owner % ny, 0, keepdims=False)

    early = ring(
        block(yi + ny - 1, 0, y_half),
        block(yi + 1, y_half, y_rows),
        lambda y_owner: block(y_owner, 0, y_half),
        lambda y_owner: block(y_owner, y_half, y_rows),
    )
    nxh = lax.axis_size("xh")
    own_block = pick(late_sum)(yi)
    late_kept = own_block[:, :width]
    late_came = lax.ppermute(own_block[:, width:], "xh", SWAP)
    for hop in range(1, ny):
        to_owner = [(i, (i + hop) % ny) for i in range(ny)]
        to_partner = [
            (h * ny + i, (nxh - 1 - h) * ny + (i + hop) % ny)
            for h in range(nxh)
            for i in range(ny)
        ]
        block_out = pick(late_sum)(yi + hop)
        late_kept = late_kept + lax.ppermute(block_out[:, :width], "y", to_owner)
        late_came = late_came + lax.ppermute(block_out[:, width:], ("xh", "y"), to_partner)
    pieces = [pair_sum(early[0]), pair_sum(early[1])]

    kept = [piece[:, :width] for piece in pieces] + [late_kept]
    came = [lax.ppermute(piece[:, width:], "xh", SWAP) for piece in pieces] + [late_came]

    def slab_group(parts):
        early = jnp.concatenate(parts[:2], axis=0).reshape(nz, y_cut, width)
        late_rows = jnp.concatenate(parts[2:], axis=0).reshape(nz, TB - y_cut, width)
        return jnp.concatenate([early, late_rows], axis=1).reshape(nz * TB, width)

    kept, came = slab_group(kept), slab_group(came)
    first = jnp.concatenate([kept, came], axis=0)
    second = jnp.concatenate([came, kept], axis=0)
    return jnp.where(xh == 0, first, second)


def solution(mesh):
    n_loop, n_long = mesh.devices.shape
    fine = Mesh(
        mesh.devices.reshape(2, n_loop // 2, n_long // 4, 2, 2), LOOP_AXES + LONG_AXES
    )
    placed = P(LONG_AXES, LOOP_AXES)
    return jax.shard_map(
        local,
        mesh=fine,
        in_specs=(placed, placed, P()),
        out_specs=placed,
        check_vma=False,
    )
```

```python
import jax
import jax.numpy as jnp
from jax import lax
from jax.sharding import Mesh
from jax.sharding import PartitionSpec as P

TB = 50
LOOP_AXES = ("xh", "z")
LONG_AXES = ("y", "xl", "c")
SWAP = [(0, 1), (1, 0)]


def local(amplitudes, integrals, owner):
    nz = lax.axis_size("z")
    ny = lax.axis_size("y")
    nxl = lax.axis_size("xl")
    kc = integrals.shape[0]
    width = amplitudes.shape[1]
    tiles_slab = integrals.shape[1] // TB
    xh = lax.axis_index("xh")
    yi = lax.axis_index("y")
    xi = lax.axis_index("xl")
    core = lax.axis_index("c")
    slab = xh * nz + lax.axis_index("z")

    slab_owner = lax.dynamic_slice(owner, (slab * tiles_slab,), (tiles_slab,))
    position = jnp.argsort(slab_owner).reshape(tiles_slab // 2, 2)
    tiles = integrals.T.reshape(tiles_slab, TB, kc)
    mine = jnp.take(tiles, position[:, core], axis=0)
    theirs = jnp.take(tiles, position[:, 1 - core], axis=0)
    from_sibling = lax.ppermute(theirs, "c", SWAP)
    own_owners = jnp.stack([mine, from_sibling], axis=2)
    y_cut = TB * 14 // 25
    gathered = lax.all_gather(own_owners[:, :y_cut], "z", axis=1, tiled=True)
    y_rows = gathered.shape[1]
    by_y = gathered.reshape(ny, nxl, y_rows, 2, kc)

    amp = jnp.concatenate([amplitudes, lax.ppermute(amplitudes, "xh", SWAP)], axis=1)
    late_rows, amp = lax.optimization_barrier((own_owners[:, y_cut:], amp))
    gathered_late = lax.all_gather(late_rows, "z", axis=1, tiled=True)
    amp = jnp.stack([amp, lax.ppermute(amp, "c", SWAP)], axis=0)

    def block(y_owner, low, high):
        lhs = lax.dynamic_index_in_dim(by_y, y_owner % ny, 0, keepdims=False)
        product = lax.dot_general(
            lhs[:, low:high], amp, (((2, 3), (0, 1)), ((), ())),
            preferred_element_type=jnp.float32,
        )
        return lax.optimization_barrier(product)

    to_next = [(i, (i + 1) % ny) for i in range(ny)]
    to_prev = [(i, (i - 1) % ny) for i in range(ny)]

    def ring(first_ahead, first_back, next_ahead, next_back):
        acc_ahead, acc_back = first_ahead, first_back
        for step in range(ny - 1):
            got_ahead = lax.ppermute(acc_ahead, "y", to_next)
            got_back = lax.ppermute(acc_back, "y", to_prev)
            acc_ahead = got_ahead + next_ahead(yi + 2 * ny - 2 - step)
            acc_back = got_back + next_back(yi + 2 + step)
        return acc_ahead, acc_back

    def pair_sum(acc):
        here = lax.dynamic_index_in_dim(acc, xi, 0, keepdims=False)
        there = lax.dynamic_index_in_dim(acc, 1 - xi, 0, keepdims=False)
        return here + lax.ppermute(there, "xl", SWAP)

    y_half = y_rows // 2
    x_rows = gathered_late.shape[1]
    late_by_xl = gathered_late.reshape(ny, nxl, x_rows, 2, kc)

    def late_block(x_owner):
        lhs = lax.dynamic_index_in_dim(late_by_xl, x_owner, 1, keepdims=False)
        product = lax.dot_general(
            lhs, amp, (((2, 3), (0, 1)), ((), ())), preferred_element_type=jnp.float32
        )
        return lax.optimization_barrier(product)

    late_there = late_block(1 - xi)
    late_here = late_block(xi)
    cut_rows = 8 * (x_rows // 16)
    late_parts = [
        late_here[:, rows] + lax.ppermute(late_there[:, rows], "xl", SWAP)
        for rows in (slice(0, cut_rows), slice(cut_rows, x_rows))
    ]

    def pick(parts):
        return lambda y_owner: lax.dynamic_index_in_dim(parts, y_owner % ny, 0, keepdims=False)

    early = ring(
        block(yi + ny - 1, 0, y_half),
        block(yi + 1, y_half, y_rows),
        lambda y_owner: block(y_owner, 0, y_half),
        lambda y_owner: block(y_owner, y_half, y_rows),
    )
    pieces = [pair_sum(early[0]), pair_sum(early[1])]
    for late_sum in late_parts:
        late_done = pick(late_sum)(yi)
        for hop in range(1, ny):
            to_owner = [(i, (i + hop) % ny) for i in range(ny)]
            late_done = late_done + lax.ppermute(pick(late_sum)(yi + hop), "y", to_owner)
        pieces.append(late_done)

    kept = [piece[:, :width] for piece in pieces]
    came = [lax.ppermute(piece[:, width:], "xh", SWAP) for piece in pieces]

    def slab_group(parts):
        early = jnp.concatenate(parts[:2], axis=0).reshape(nz, y_cut, width)
        late_rows = jnp.concatenate(parts[2:], axis=0).reshape(nz, TB - y_cut, width)
        return jnp.concatenate([early, late_rows], axis=1).reshape(nz * TB, width)

    kept, came = slab_group(kept), slab_group(came)
    first = jnp.concatenate([kept, came], axis=0)
    second = jnp.concatenate([came, kept], axis=0)
    return jnp.where(xh == 0, first, second)


def solution(mesh):
    n_loop, n_long = mesh.devices.shape
    fine = Mesh(
        mesh.devices.reshape(2, n_loop // 2, n_long // 4, 2, 2), LOOP_AXES + LONG_AXES
    )
    placed = P(LONG_AXES, LOOP_AXES)
    return jax.shard_map(
        local,
        mesh=fine,
        in_specs=(placed, placed, P()),
        out_specs=placed,
        check_vma=False,
    )
```

```python
import jax
import jax.numpy as jnp
from jax import lax
from jax.sharding import Mesh
from jax.sharding import PartitionSpec as P

TB = 50
LOOP_AXES = ("xh", "z")
LONG_AXES = ("y", "xl", "c")
SWAP = [(0, 1), (1, 0)]


def local(amplitudes, integrals, owner):
    nz = lax.axis_size("z")
    ny = lax.axis_size("y")
    nxl = lax.axis_size("xl")
    kc = integrals.shape[0]
    width = amplitudes.shape[1]
    tiles_slab = integrals.shape[1] // TB
    xh = lax.axis_index("xh")
    yi = lax.axis_index("y")
    xi = lax.axis_index("xl")
    core = lax.axis_index("c")
    slab = xh * nz + lax.axis_index("z")

    slab_owner = lax.dynamic_slice(owner, (slab * tiles_slab,), (tiles_slab,))
    position = jnp.argsort(slab_owner).reshape(tiles_slab // 2, 2)
    tiles = integrals.T.reshape(tiles_slab, TB, kc)
    mine = jnp.take(tiles, position[:, core], axis=0)
    theirs = jnp.take(tiles, position[:, 1 - core], axis=0)
    from_sibling = lax.ppermute(theirs, "c", SWAP)
    own_owners = jnp.stack([mine, from_sibling], axis=2)
    y_cut = TB * 14 // 25
    gathered = lax.all_gather(own_owners[:, :y_cut], "z", axis=1, tiled=True)
    y_rows = gathered.shape[1]
    by_y = gathered.reshape(ny, nxl, y_rows, 2, kc)

    amp = jnp.concatenate([amplitudes, lax.ppermute(amplitudes, "xh", SWAP)], axis=1)
    late_rows, amp = lax.optimization_barrier((own_owners[:, y_cut:], amp))
    gathered_late = lax.all_gather(late_rows, "z", axis=1, tiled=True)
    amp = jnp.stack([amp, lax.ppermute(amp, "c", SWAP)], axis=0)

    def block(y_owner, low, high):
        lhs = lax.dynamic_index_in_dim(by_y, y_owner % ny, 0, keepdims=False)
        product = lax.dot_general(
            lhs[:, low:high], amp, (((2, 3), (0, 1)), ((), ())),
            preferred_element_type=jnp.float32,
        )
        return lax.optimization_barrier(product)

    to_next = [(i, (i + 1) % ny) for i in range(ny)]
    to_prev = [(i, (i - 1) % ny) for i in range(ny)]

    def ring(first_ahead, first_back, next_ahead, next_back):
        acc_ahead, acc_back = first_ahead, first_back
        for step in range(ny - 1):
            got_ahead = lax.ppermute(acc_ahead, "y", to_next)
            got_back = lax.ppermute(acc_back, "y", to_prev)
            acc_ahead = got_ahead + next_ahead(yi + 2 * ny - 2 - step)
            acc_back = got_back + next_back(yi + 2 + step)
        return acc_ahead, acc_back

    def pair_sum(acc):
        here = lax.dynamic_index_in_dim(acc, xi, 0, keepdims=False)
        there = lax.dynamic_index_in_dim(acc, 1 - xi, 0, keepdims=False)
        return here + lax.ppermute(there, "xl", SWAP)

    y_half = y_rows // 2
    x_rows = gathered_late.shape[1]
    late_by_xl = gathered_late.reshape(ny, nxl, x_rows, 2, kc)

    def late_block(x_owner):
        lhs = lax.dynamic_index_in_dim(late_by_xl, x_owner, 1, keepdims=False)
        product = lax.dot_general(
            lhs, amp, (((2, 3), (0, 1)), ((), ())), preferred_element_type=jnp.float32
        )
        return lax.optimization_barrier(product)

    late_there = late_block(1 - xi)
    late_sum = late_block(xi) + lax.ppermute(late_there, "xl", SWAP)

    def pick(parts):
        return lambda y_owner: lax.dynamic_index_in_dim(parts, y_owner % ny, 0, keepdims=False)

    early = ring(
        block(yi + ny - 1, 0, y_half),
        block(yi + 1, y_half, y_rows),
        lambda y_owner: block(y_owner, 0, y_half),
        lambda y_owner: block(y_owner, y_half, y_rows),
    )
    late_done = pick(late_sum)(yi)
    for hop in range(1, ny):
        to_owner = [(i, (i + hop) % ny) for i in range(ny)]
        late_done = late_done + lax.ppermute(pick(late_sum)(yi + hop), "y", to_owner)
    pieces = [pair_sum(jnp.concatenate(early, axis=1)), late_done]

    kept = [piece[:, :width] for piece in pieces]
    came = [lax.ppermute(piece[:, width:], "xh", SWAP) for piece in pieces]

    def slab_group(parts):
        early = parts[0].reshape(nz, y_cut, width)
        late_rows = parts[1].reshape(nz, TB - y_cut, width)
        return jnp.concatenate([early, late_rows], axis=1).reshape(nz * TB, width)

    kept, came = slab_group(kept), slab_group(came)
    first = jnp.concatenate([kept, came], axis=0)
    second = jnp.concatenate([came, kept], axis=0)
    return jnp.where(xh == 0, first, second)


def solution(mesh):
    n_loop, n_long = mesh.devices.shape
    fine = Mesh(
        mesh.devices.reshape(2, n_loop // 2, n_long // 4, 2, 2), LOOP_AXES + LONG_AXES
    )
    placed = P(LONG_AXES, LOOP_AXES)
    return jax.shard_map(
        local,
        mesh=fine,
        in_specs=(placed, placed, P()),
        out_specs=placed,
        check_vma=False,
    )
```

```python
import jax
import jax.numpy as jnp
from jax import lax
from jax.sharding import Mesh
from jax.sharding import PartitionSpec as P

TB = 50
LOOP_AXES = ("xh", "z")
LONG_AXES = ("y", "xl", "c")
SWAP = [(0, 1), (1, 0)]


def local(amplitudes, integrals, owner):
    nz = lax.axis_size("z")
    ny = lax.axis_size("y")
    nxl = lax.axis_size("xl")
    kc = integrals.shape[0]
    width = amplitudes.shape[1]
    tiles_slab = integrals.shape[1] // TB
    xh = lax.axis_index("xh")
    yi = lax.axis_index("y")
    xi = lax.axis_index("xl")
    core = lax.axis_index("c")
    slab = xh * nz + lax.axis_index("z")

    slab_owner = lax.dynamic_slice(owner, (slab * tiles_slab,), (tiles_slab,))
    position = jnp.argsort(slab_owner).reshape(tiles_slab // 2, 2)
    tiles = integrals.T.reshape(tiles_slab, TB, kc)
    mine = jnp.take(tiles, position[:, core], axis=0)
    theirs = jnp.take(tiles, position[:, 1 - core], axis=0)
    from_sibling = lax.ppermute(theirs, "c", SWAP)
    own_owners = jnp.stack([mine, from_sibling], axis=2)
    y_cut = TB * 14 // 25
    gathered = lax.all_gather(own_owners[:, :y_cut], "z", axis=1, tiled=True)
    y_rows = gathered.shape[1]
    by_y = gathered.reshape(ny, nxl, y_rows, 2, kc)

    amp = jnp.concatenate([amplitudes, lax.ppermute(amplitudes, "xh", SWAP)], axis=1)
    late_rows, amp = lax.optimization_barrier((own_owners[:, y_cut:], amp))
    gathered_late = lax.all_gather(late_rows, "z", axis=1, tiled=True)
    amp = jnp.stack([amp, lax.ppermute(amp, "c", SWAP)], axis=0)

    def block(y_owner, low, high):
        lhs = lax.dynamic_index_in_dim(by_y, y_owner % ny, 0, keepdims=False)
        product = lax.dot_general(
            lhs[:, low:high], amp, (((2, 3), (0, 1)), ((), ())),
            preferred_element_type=jnp.float32,
        )
        return lax.optimization_barrier(product)

    to_next = [(i, (i + 1) % ny) for i in range(ny)]
    to_prev = [(i, (i - 1) % ny) for i in range(ny)]

    def ring(first_ahead, first_back, next_ahead, next_back):
        acc_ahead, acc_back = first_ahead, first_back
        for step in range(ny - 1):
            got_ahead = lax.ppermute(acc_ahead, "y", to_next)
            got_back = lax.ppermute(acc_back, "y", to_prev)
            acc_ahead = got_ahead + next_ahead(yi + 2 * ny - 2 - step)
            acc_back = got_back + next_back(yi + 2 + step)
        return acc_ahead, acc_back

    def pair_sum(acc):
        here = lax.dynamic_index_in_dim(acc, xi, 0, keepdims=False)
        there = lax.dynamic_index_in_dim(acc, 1 - xi, 0, keepdims=False)
        return here + lax.ppermute(there, "xl", SWAP)

    y_half = y_rows // 2
    x_rows = gathered_late.shape[1]
    late_by_xl = gathered_late.reshape(ny, nxl, x_rows, 2, kc)

    def late_block(x_owner):
        lhs = lax.dynamic_index_in_dim(late_by_xl, x_owner, 1, keepdims=False)
        product = lax.dot_general(
            lhs, amp, (((2, 3), (0, 1)), ((), ())), preferred_element_type=jnp.float32
        )
        return lax.optimization_barrier(product)

    late_there = late_block(1 - xi)
    late_sum = late_block(xi) + lax.ppermute(late_there, "xl", SWAP)

    def pick(parts):
        return lambda y_owner: lax.dynamic_index_in_dim(parts, y_owner % ny, 0, keepdims=False)

    early = ring(
        block(yi + ny - 1, 0, y_half),
        block(yi + 1, y_half, y_rows),
        lambda y_owner: block(y_owner, 0, y_half),
        lambda y_owner: block(y_owner, y_half, y_rows),
    )
    late_done = pick(late_sum)(yi)
    for hop in range(1, ny):
        to_owner = [(i, (i + hop) % ny) for i in range(ny)]
        late_done = late_done + lax.ppermute(pick(late_sum)(yi + hop), "y", to_owner)
    pieces = [pair_sum(early[0]), pair_sum(early[1]), late_done]

    kept = [piece[:, :width] for piece in pieces]
    came = [lax.ppermute(piece[:, width:], "xh", SWAP) for piece in pieces]

    def slab_group(parts):
        early = jnp.concatenate(parts[:2], axis=0).reshape(nz, y_cut, width)
        late_rows = jnp.concatenate(parts[2:], axis=0).reshape(nz, TB - y_cut, width)
        return jnp.concatenate([early, late_rows], axis=1).reshape(nz * TB, width)

    kept, came = slab_group(kept), slab_group(came)
    both = jnp.concatenate([kept, came, kept], axis=0)
    return lax.dynamic_slice_in_dim(both, xh * kept.shape[0], 2 * kept.shape[0], 0)


def solution(mesh):
    n_loop, n_long = mesh.devices.shape
    fine = Mesh(
        mesh.devices.reshape(2, n_loop // 2, n_long // 4, 2, 2), LOOP_AXES + LONG_AXES
    )
    placed = P(LONG_AXES, LOOP_AXES)
    return jax.shard_map(
        local,
        mesh=fine,
        in_specs=(placed, placed, P()),
        out_specs=placed,
        check_vma=False,
    )
```

```python
import jax
import jax.numpy as jnp
from jax import lax
from jax.sharding import Mesh
from jax.sharding import PartitionSpec as P

TB = 50
LOOP_AXES = ("xh", "z")
LONG_AXES = ("y", "xl", "c")
SWAP = [(0, 1), (1, 0)]


def local(amplitudes, integrals, owner):
    nz = lax.axis_size("z")
    ny = lax.axis_size("y")
    nxl = lax.axis_size("xl")
    kc = integrals.shape[0]
    width = amplitudes.shape[1]
    tiles_slab = integrals.shape[1] // TB
    xh = lax.axis_index("xh")
    yi = lax.axis_index("y")
    xi = lax.axis_index("xl")
    core = lax.axis_index("c")
    slab = xh * nz + lax.axis_index("z")

    slab_owner = lax.dynamic_slice(owner, (slab * tiles_slab,), (tiles_slab,))
    position = jnp.argsort(slab_owner).reshape(tiles_slab // 2, 2)
    tiles = integrals.T.reshape(tiles_slab, TB, kc)
    mine = jnp.take(tiles, position[:, core], axis=0)
    theirs = jnp.take(tiles, position[:, 1 - core], axis=0)
    from_sibling = lax.ppermute(theirs, "c", SWAP)
    own_owners = jnp.stack([mine, from_sibling], axis=2)
    y_cut = TB * 14 // 25
    gathered = lax.all_gather(own_owners[:, :y_cut], "z", axis=1, tiled=True)
    y_rows = gathered.shape[1]
    by_y = gathered.reshape(ny, nxl, y_rows, 2, kc)

    sibling_own = lax.ppermute(amplitudes, "c", SWAP)
    partner = lax.ppermute(amplitudes, "xh", SWAP)
    late_rows, partner = lax.optimization_barrier((own_owners[:, y_cut:], partner))
    gathered_late = lax.all_gather(late_rows, "z", axis=1, tiled=True)
    sibling_partner = lax.ppermute(partner, "c", SWAP)
    amp = jnp.stack(
        [
            jnp.concatenate([amplitudes, partner], axis=1),
            jnp.concatenate([sibling_own, sibling_partner], axis=1),
        ],
        axis=0,
    )

    def block(y_owner, low, high):
        lhs = lax.dynamic_index_in_dim(by_y, y_owner % ny, 0, keepdims=False)
        product = lax.dot_general(
            lhs[:, low:high], amp, (((2, 3), (0, 1)), ((), ())),
            preferred_element_type=jnp.float32,
        )
        return lax.optimization_barrier(product)

    to_next = [(i, (i + 1) % ny) for i in range(ny)]
    to_prev = [(i, (i - 1) % ny) for i in range(ny)]

    def ring(first_ahead, first_back, next_ahead, next_back):
        acc_ahead, acc_back = first_ahead, first_back
        for step in range(ny - 1):
            got_ahead = lax.ppermute(acc_ahead, "y", to_next)
            got_back = lax.ppermute(acc_back, "y", to_prev)
            acc_ahead = got_ahead + next_ahead(yi + 2 * ny - 2 - step)
            acc_back = got_back + next_back(yi + 2 + step)
        return acc_ahead, acc_back

    def pair_sum(acc):
        here = lax.dynamic_index_in_dim(acc, xi, 0, keepdims=False)
        there = lax.dynamic_index_in_dim(acc, 1 - xi, 0, keepdims=False)
        return here + lax.ppermute(there, "xl", SWAP)

    y_half = y_rows // 2
    x_rows = gathered_late.shape[1]
    late_by_xl = gathered_late.reshape(ny, nxl, x_rows, 2, kc)

    def late_block(x_owner):
        lhs = lax.dynamic_index_in_dim(late_by_xl, x_owner, 1, keepdims=False)
        product = lax.dot_general(
            lhs, amp, (((2, 3), (0, 1)), ((), ())), preferred_element_type=jnp.float32
        )
        return lax.optimization_barrier(product)

    late_there = late_block(1 - xi)
    late_sum = late_block(xi) + lax.ppermute(late_there, "xl", SWAP)

    def pick(parts):
        return lambda y_owner: lax.dynamic_index_in_dim(parts, y_owner % ny, 0, keepdims=False)

    early = ring(
        block(yi + ny - 1, 0, y_half),
        block(yi + 1, y_half, y_rows),
        lambda y_owner: block(y_owner, 0, y_half),
        lambda y_owner: block(y_owner, y_half, y_rows),
    )
    late_done = pick(late_sum)(yi)
    for hop in range(1, ny):
        to_owner = [(i, (i + hop) % ny) for i in range(ny)]
        late_done = late_done + lax.ppermute(pick(late_sum)(yi + hop), "y", to_owner)
    pieces = [pair_sum(early[0]), pair_sum(early[1]), late_done]

    kept = [piece[:, :width] for piece in pieces]
    came = [lax.ppermute(piece[:, width:], "xh", SWAP) for piece in pieces]

    def slab_group(parts):
        early = jnp.concatenate(parts[:2], axis=0).reshape(nz, y_cut, width)
        late_rows = jnp.concatenate(parts[2:], axis=0).reshape(nz, TB - y_cut, width)
        return jnp.concatenate([early, late_rows], axis=1).reshape(nz * TB, width)

    kept, came = slab_group(kept), slab_group(came)
    first = jnp.concatenate([kept, came], axis=0)
    second = jnp.concatenate([came, kept], axis=0)
    return jnp.where(xh == 0, first, second)


def solution(mesh):
    n_loop, n_long = mesh.devices.shape
    fine = Mesh(
        mesh.devices.reshape(2, n_loop // 2, n_long // 4, 2, 2), LOOP_AXES + LONG_AXES
    )
    placed = P(LONG_AXES, LOOP_AXES)
    return jax.shard_map(
        local,
        mesh=fine,
        in_specs=(placed, placed, P()),
        out_specs=placed,
        check_vma=False,
    )
```
